512 devices in a mesh: ctx: 64 (over y, z_lo, core), dp: 8 (over z_hi, x).
Axes of the slice: x: 4, y: 8, z: 8 (z_hi: 2, z_lo: 4; z = z_hi * 4 + z_lo), core: 2. Of those that a mesh axis runs over, the one named last changes fastest.
Arguments:
- features: bfloat16 [8, 12288, 1536], P('dp', 'ctx'), may hold values from -6 to 6
- bottleneck: bfloat16 [8, 12288, 384], P('dp', 'ctx'), may hold values from -6 to 6
- node_noise: bfloat16 [8, 12288, 1536], P('dp', 'ctx'), may hold values from -6 to 6
- targets: bfloat16 [8, 12288, 1536], P('dp', 'ctx'), may hold values from -15 to 15
- entry_weight: bfloat16 [384, 1536], P('ctx'), may hold values from -0.3125 to 0.3125
- conv_filters: bfloat16 [3, 1536, 384], P(None, None, 'ctx'), may hold values from -0.09375 to 0.09375
- exit_weight: bfloat16 [384, 1536], P('ctx'), may hold values from -0.3125 to 0.3125
Outputs:
- blended: bfloat16 [8, 12288, 1536], P('dp', 'ctx')
- estimate: float32 [384, 1536], P('ctx')
The draws below stay inside these ranges and needn't reach their ends.
All inputs are finite; a program needn't handle non-finite values.
Results may differ from the reference program's by a relative error of at most 0.015.
The reference program's roundings to bfloat16 on the way count: a program that leaves them out, or rounds other values in their place, can miss the bound.
Values may be sent and summed in bfloat16 or wider, within the bound.
No kernel may reach another device: no remote copies, remote signals or barrier semaphores. Data moves between devices by JAX's collectives and lax.ppermute only.
A program may use at most 64 MiB of HBM per device.

```python
import jax
import jax.numpy as jnp
from jax import lax

CH = 1536
BOT = 384
DILATION = 32
BINS = 12288
SEQS = 8


def draw_targets(key, part):
    position = jnp.arange(BINS, dtype=jnp.float32)
    ramp = 0.5 + 4.5 * position / BINS
    values = jnp.clip(jax.random.normal(key, (SEQS, BINS, CH), jnp.float32), -3.0, 3.0)
    return (values * ramp[None, :, None]).astype(jnp.bfloat16)


def level_of(own_key, extent, shards, low, top_value):
    def one(axis_at, parts):
        heights = jax.random.uniform(jax.random.fold_in(jax.random.fold_in(own_key, 6), axis_at), (parts,), jnp.float32, low / len(shards), top_value / len(shards))
        return jnp.repeat(jnp.exp(heights), extent[axis_at] // parts).reshape((-1,) + (1,) * (len(extent) - axis_at - 1))

    level = one(*shards[0])
    for cut in shards[1:]:
        level = level * one(*cut)
    return level


def scatter_about(rng, dims, scale, limit, shards=(), held_as=jnp.bfloat16):
    factor_of = level_of(rng, dims, shards, -0.22, 0.18) if shards else 1.0
    drawn = jax.random.normal(rng, dims, jnp.float32) * scale * factor_of
    return jnp.minimum(jnp.maximum(drawn, -limit), limit).astype(held_as)


def setup_inputs(seed: int = 0) -> dict:
    seeds = jax.random.split(jax.random.key(seed), 8)
    features = scatter_about(seeds[0], (SEQS, BINS, CH), 1.0, 6.0, ((0, 8), (1, 64)))
    bottleneck = scatter_about(seeds[1], (SEQS, BINS, BOT), 1.0, 6.0, ((0, 8), (1, 64)))
    node_noise = scatter_about(seeds[2], (SEQS, BINS, CH), 1.0, 6.0, ((0, 8), (1, 64)))
    targets = draw_targets(jax.random.fold_in(seeds[7], 71), 0)
    entry_weight = scatter_about(seeds[4], (BOT, CH), BOT ** -0.5, 0.3125, ((0, 64),))
    conv_filters = scatter_about(seeds[5], (3, CH, BOT), (3 * CH) ** -0.5, 0.09375, ((2, 64),))
    exit_weight = scatter_about(seeds[6], (BOT, CH), BOT ** -0.5, 0.3125, ((0, 64),))
    return {"features": features, "bottleneck": bottleneck, "node_noise": node_noise, "targets": targets, "entry_weight": entry_weight, "conv_filters": conv_filters, "exit_weight": exit_weight}


NOISE_SCALE = 0.1


def second_block(state, conv_filters, exit_weight):
    activated = jax.nn.gelu(state).astype(jnp.bfloat16)
    padded = jnp.pad(activated, ((DILATION, DILATION), (0, 0)))
    length = state.shape[0]
    mixed = jnp.dot(padded[0:length], conv_filters[0], preferred_element_type=jnp.float32)
    mixed = mixed + jnp.dot(padded[DILATION:DILATION + length], conv_filters[1], preferred_element_type=jnp.float32)
    mixed = mixed + jnp.dot(padded[2 * DILATION:2 * DILATION + length], conv_filters[2], preferred_element_type=jnp.float32)
    inner = jax.nn.gelu(mixed).astype(jnp.bfloat16)
    return state + jnp.dot(inner, exit_weight, preferred_element_type=jnp.float32)


def reference(features, bottleneck, node_noise, targets, entry_weight, conv_filters, exit_weight):
    def one_sequence(items):
        feats, bottle, jitter, goal = items
        baseline = feats.astype(jnp.float32) + jnp.dot(bottle, entry_weight, preferred_element_type=jnp.float32)
        offset = jitter.astype(jnp.float32) * NOISE_SCALE
        upper = second_block(baseline + offset, conv_filters, exit_weight)
        lower = second_block(baseline - offset, conv_filters, exit_weight)
        blended = ((upper + lower) * 0.5).astype(jnp.bfloat16)
        gap = jnp.sum((upper - lower) * (upper + lower - 2.0 * goal.astype(jnp.float32))) / (BINS * CH)
        summed = lax.dot_general(bottle, jitter, (((0,), (0,)), ((), ())), preferred_element_type=jnp.float32)
        return blended, (gap / (2.0 * NOISE_SCALE)) * summed

    blended_all, weighted = lax.map(one_sequence, (features, bottleneck, node_noise, targets))
    return blended_all, jnp.sum(weighted, axis=0)
```

```python
import jax
import jax.numpy as jnp
from jax import lax
from jax.sharding import Mesh
from jax.sharding import PartitionSpec as P

DILATION = 32

NOISE_SCALE = 0.1

CTX = ("y", "zl", "c")
DP = ("zh", "x")


def _size(axes):
    n = 1
    for a in axes:
        n *= lax.axis_size(a)
    return n


def body(features, bottleneck, node_noise, targets, entry_weight, conv_filters, exit_weight):
    feats = features[0]
    bottle = bottleneck[0]
    jitter = node_noise[0]
    goal = targets[0].astype(jnp.float32)
    rows, chans = feats.shape
    bot = bottle.shape[1]
    n_ctx = _size(CTX)
    ny, nz, nc = (lax.axis_size(a) for a in CTX)
    shard = entry_weight.shape[0]

    bottle_perm = (
        bottle.reshape(rows, ny, nz, nc, shard).transpose(0, 3, 2, 1, 4).reshape(rows, bot)
    )
    summed = lax.dot_general(
        bottle_perm, jitter, (((0,), (0,)), ((), ())), preferred_element_type=jnp.float32
    )
    for axis in ("c", "zl", "y"):
        summed = lax.psum_scatter(summed, axis, scatter_dimension=0, tiled=True)

    conv_rows = conv_filters.transpose(2, 0, 1).reshape(shard, -1)
    packed = jnp.concatenate([entry_weight, conv_rows, exit_weight], axis=1)
    packed = lax.all_gather(packed, "y", axis=0, tiled=False)
    packed = lax.all_gather(packed, "zl", axis=1, tiled=False)
    packed = lax.all_gather(packed, "c", axis=2, tiled=False)
    packed = packed.reshape(n_ctx * shard, -1)
    w_entry = packed[:, :chans]
    w_conv = packed[:, chans : 4 * chans].reshape(bot, 3, chans)
    w_exit = packed[:, 4 * chans :]

    spacing = DILATION
    edge_in = jnp.concatenate([feats, bottle, jitter], axis=1)
    pairs_up = [(i, i + 1) for i in range(n_ctx - 1)]
    pairs_down = [(i + 1, i) for i in range(n_ctx - 1)]
    from_prev = lax.ppermute(edge_in[rows - spacing :], CTX, pairs_up)
    from_next = lax.ppermute(edge_in[:spacing], CTX, pairs_down)
    ext = jnp.concatenate([from_prev, edge_in, from_next], axis=0)
    ext_feats = ext[:, :chans]
    ext_bottle = ext[:, chans : chans + bot]
    ext_jitter = ext[:, chans + bot :]

    baseline = ext_feats.astype(jnp.float32) + jnp.dot(
        ext_bottle, w_entry, preferred_element_type=jnp.float32
    )
    offset = ext_jitter.astype(jnp.float32) * NOISE_SCALE
    state = jnp.stack([baseline + offset, baseline - offset])
    activated = jax.nn.gelu(state).astype(jnp.bfloat16)
    mixed = None
    for k in range(3):
        term = lax.dot_general(
            activated[:, k * spacing : k * spacing + rows],
            w_conv[:, k, :],
            (((2,), (1,)), ((), ())),
            preferred_element_type=jnp.float32,
        )
        mixed = term if mixed is None else mixed + term
    inner = jax.nn.gelu(mixed).astype(jnp.bfloat16)
    outs = state[:, spacing : spacing + rows] + jnp.dot(
        inner, w_exit, preferred_element_type=jnp.float32
    )
    upper = outs[0]
    lower = outs[1]
    blended = ((upper + lower) * 0.5).astype(jnp.bfloat16)[None]
    local_gap = jnp.sum((upper - lower) * (upper + lower - 2.0 * goal)) / (rows * n_ctx * chans)
    gap = local_gap
    for axis in ("c", "zl", "y"):
        gap = lax.psum(gap, axis)
    factor = gap / (2.0 * NOISE_SCALE)
    estimate = factor * summed
    for axis in ("x", "zh"):
        estimate = lax.psum(estimate, axis)
    return (blended, estimate)


def solution(mesh):
    ctx_n, dp_n = mesh.devices.shape
    devices = mesh.devices.reshape(8, ctx_n // 16, 2, dp_n // 4, 4)
    fine = Mesh(devices, CTX + DP)
    return jax.shard_map(
        body,
        mesh=fine,
        in_specs=(
            P(DP, CTX, None),
            P(DP, CTX, None),
            P(DP, CTX, None),
            P(DP, CTX, None),
            P(CTX, None),
            P(None, None, CTX),
            P(CTX, None),
        ),
        out_specs=(P(DP, CTX, None), P(CTX, None)),
        check_vma=False,
    )
```

```python
import jax
import jax.numpy as jnp
from jax import lax
from jax.sharding import Mesh
from jax.sharding import PartitionSpec as P

DILATION = 32

NOISE_SCALE = 0.1

CTX = ("y", "zl", "c")
DP = ("zh", "x")


def _size(axes):
    n = 1
    for a in axes:
        n *= lax.axis_size(a)
    return n


def body(features, bottleneck, node_noise, targets, entry_weight, conv_filters, exit_weight):
    feats = features[0]
    bottle = bottleneck[0]
    jitter = node_noise[0]
    goal = targets[0].astype(jnp.float32)
    rows, chans = feats.shape
    bot = bottle.shape[1]
    n_ctx = _size(CTX)
    ny, nz, nc = (lax.axis_size(a) for a in CTX)
    shard = entry_weight.shape[0]

    bottle_perm = (
        bottle.reshape(rows, ny, nz, nc, shard).transpose(0, 3, 2, 1, 4).reshape(rows, bot)
    )
    summed = lax.dot_general(
        bottle_perm, jitter, (((0,), (0,)), ((), ())), preferred_element_type=jnp.float32
    )
    for axis in ("c", "zl", "y"):
        summed = lax.psum_scatter(summed, axis, scatter_dimension=0, tiled=True)
    summed_all = lax.all_gather(summed, DP, axis=0, tiled=False)

    n_dp = _size(DP)
    me_dp = lax.axis_index("zh") * lax.axis_size("x") + lax.axis_index("x")
    conv_rows = conv_filters.transpose(2, 0, 1).reshape(shard, -1)
    parts = [
        lax.dynamic_slice_in_dim(w.reshape(shard, n_dp, -1), me_dp, 1, axis=1)[:, 0]
        for w in (entry_weight, conv_rows, exit_weight)
    ]
    piece = jnp.concatenate(parts, axis=1)
    packed = lax.all_gather(piece, CTX + DP, axis=0, tiled=False)
    packed = packed.reshape(n_ctx, n_dp, shard, -1)
    cw = chans // n_dp
    w_entry = packed[..., :cw].transpose(0, 2, 1, 3).reshape(n_ctx * shard, chans)
    w_conv = packed[..., cw : 4 * cw].transpose(0, 2, 1, 3).reshape(bot, 3, chans)
    w_exit = packed[..., 4 * cw :].transpose(0, 2, 1, 3).reshape(n_ctx * shard, chans)

    spacing = DILATION
    edge_in = jnp.concatenate([feats, bottle, jitter], axis=1)
    pairs_up = [(i, i + 1) for i in range(n_ctx - 1)]
    pairs_down = [(i + 1, i) for i in range(n_ctx - 1)]
    from_prev = lax.ppermute(edge_in[rows - spacing :], CTX, pairs_up)
    from_next = lax.ppermute(edge_in[:spacing], CTX, pairs_down)
    ext = jnp.concatenate([from_prev, edge_in, from_next], axis=0)
    ext_feats = ext[:, :chans]
    ext_bottle = ext[:, chans : chans + bot]
    ext_jitter = ext[:, chans + bot :]

    baseline = ext_feats.astype(jnp.float32) + jnp.dot(
        ext_bottle, w_entry, preferred_element_type=jnp.float32
    )
    offset = ext_jitter.astype(jnp.float32) * NOISE_SCALE
    state = jnp.stack([baseline + offset, baseline - offset])
    activated = jax.nn.gelu(state).astype(jnp.bfloat16)
    mixed = None
    for k in range(3):
        term = lax.dot_general(
            activated[:, k * spacing : k * spacing + rows],
            w_conv[:, k, :],
            (((2,), (1,)), ((), ())),
            preferred_element_type=jnp.float32,
        )
        mixed = term if mixed is None else mixed + term
    inner = jax.nn.gelu(mixed).astype(jnp.bfloat16)
    outs = state[:, spacing : spacing + rows] + jnp.dot(
        inner, w_exit, preferred_element_type=jnp.float32
    )
    upper = outs[0]
    lower = outs[1]
    blended = ((upper + lower) * 0.5).astype(jnp.bfloat16)[None]
    local_gap = jnp.sum((upper - lower) * (upper + lower - 2.0 * goal)) / (rows * n_ctx * chans)
    slots = jnp.zeros((n_dp,), jnp.float32).at[me_dp].set(local_gap)
    gaps = lax.psum(slots, CTX + DP)
    factors = gaps / (2.0 * NOISE_SCALE)
    estimate = jnp.sum(factors[:, None, None] * summed_all, axis=0)
    return (blended, estimate)


def solution(mesh):
    ctx_n, dp_n = mesh.devices.shape
    devices = mesh.devices.reshape(8, ctx_n // 16, 2, dp_n // 4, 4)
    fine = Mesh(devices, CTX + DP)
    return jax.shard_map(
        body,
        mesh=fine,
        in_specs=(
            P(DP, CTX, None),
            P(DP, CTX, None),
            P(DP, CTX, None),
            P(DP, CTX, None),
            P(CTX, None),
            P(None, None, CTX),
            P(CTX, None),
        ),
        out_specs=(P(DP, CTX, None), P(CTX, None)),
        check_vma=False,
    )
```

```python
import jax
import jax.numpy as jnp
from jax import lax
from jax.sharding import Mesh
from jax.sharding import PartitionSpec as P

DILATION = 32

NOISE_SCALE = 0.1

CTX = ("y", "zl", "c")
DP = ("zh", "x")


def _size(axes):
    n = 1
    for a in axes:
        n *= lax.axis_size(a)
    return n


def _swap(x, axis, d):
    n = lax.axis_size(axis)
    return lax.ppermute(x, axis, [(i, i ^ d) for i in range(n)])


def _bit(axis, d):
    return (lax.axis_index(axis) // d) % 2


DIGITS = (("y", 4), ("y", 2), ("y", 1), ("zl", 2), ("zl", 1), ("c", 1))


def _gather_rows(piece, order):
    held = piece.reshape((1,) * len(DIGITS) + piece.shape)
    for axis, d in order:
        dim = DIGITS.index((axis, d))
        theirs = _swap(held, axis, d)
        low = jnp.concatenate([held, theirs], axis=dim)
        high = jnp.concatenate([theirs, held], axis=dim)
        held = jnp.where(_bit(axis, d) == 0, low, high)
    return held.reshape((-1,) + piece.shape[1:])


def _scatter_rows(full, order, shard):
    held = full.reshape((2,) * len(DIGITS) + (shard,) + full.shape[1:])
    for axis, d in order:
        dim = DIGITS.index((axis, d))
        mine = _bit(axis, d)
        keep = lax.dynamic_index_in_dim(held, mine, axis=dim, keepdims=True)
        give = lax.dynamic_index_in_dim(held, 1 - mine, axis=dim, keepdims=True)
        held = keep + _swap(give, axis, d)
    return held.reshape((shard,) + full.shape[1:])


def _sum_all(x, steps):
    for axis, d in steps:
        x = x + _swap(x, axis, d)
    return x


def body(features, bottleneck, node_noise, targets, entry_weight, conv_filters, exit_weight):
    feats = features[0]
    bottle = bottleneck[0]
    jitter = node_noise[0]
    goal = targets[0].astype(jnp.float32)
    rows, chans = feats.shape
    bot = bottle.shape[1]
    n_ctx = _size(CTX)
    ny, nz, nc = (lax.axis_size(a) for a in CTX)
    shard = entry_weight.shape[0]

    summed = lax.dot_general(
        bottle, jitter, (((0,), (0,)), ((), ())), preferred_element_type=jnp.float32
    )
    summed = _scatter_rows(
        summed, (("c", 1), ("zl", 1), ("zl", 2), ("y", 1), ("y", 2), ("y", 4)), shard
    )

    conv_rows = conv_filters.transpose(2, 0, 1).reshape(shard, -1)
    packed = jnp.concatenate([entry_weight, conv_rows, exit_weight], axis=1)
    packed = _gather_rows(
        packed, (("y", 4), ("y", 2), ("zl", 2), ("y", 1), ("zl", 1), ("c", 1))
    )
    w_entry = packed[:, :chans]
    w_conv = packed[:, chans : 4 * chans].reshape(bot, 3, chans)
    w_exit = packed[:, 4 * chans :]

    spacing = DILATION
    edge_in = jnp.concatenate([feats, bottle, jitter], axis=1)
    pairs_up = [(i, i + 1) for i in range(n_ctx - 1)]
    pairs_down = [(i + 1, i) for i in range(n_ctx - 1)]
    from_prev = lax.ppermute(edge_in[rows - spacing :], CTX, pairs_up)
    from_next = lax.ppermute(edge_in[:spacing], CTX, pairs_down)
    ext = jnp.concatenate([from_prev, edge_in, from_next], axis=0)
    ext_feats = ext[:, :chans]
    ext_bottle = ext[:, chans : chans + bot]
    ext_jitter = ext[:, chans + bot :]

    baseline = ext_feats.astype(jnp.float32) + jnp.dot(
        ext_bottle, w_entry, preferred_element_type=jnp.float32
    )
    offset = ext_jitter.astype(jnp.float32) * NOISE_SCALE
    state = jnp.stack([baseline + offset, baseline - offset])
    activated = jax.nn.gelu(state).astype(jnp.bfloat16)
    mixed = None
    for k in range(3):
        term = lax.dot_general(
            activated[:, k * spacing : k * spacing + rows],
            w_conv[:, k, :],
            (((2,), (1,)), ((), ())),
            preferred_element_type=jnp.float32,
        )
        mixed = term if mixed is None else mixed + term
    inner = jax.nn.gelu(mixed).astype(jnp.bfloat16)
    outs = state[:, spacing : spacing + rows] + jnp.dot(
        inner, w_exit, preferred_element_type=jnp.float32
    )
    upper = outs[0]
    lower = outs[1]
    blended = ((upper + lower) * 0.5).astype(jnp.bfloat16)[None]
    local_gap = jnp.sum((upper - lower) * (upper + lower - 2.0 * goal)) / (rows * n_ctx * chans)
    gap = _sum_all(local_gap.reshape(1), (("c", 1), ("zl", 1), ("zl", 2), ("y", 1), ("y", 2), ("y", 4)))
    factor = gap / (2.0 * NOISE_SCALE)
    estimate = _sum_all(factor * summed, (("x", 1), ("x", 2), ("zh", 1)))
    return (blended, estimate)


def solution(mesh):
    ctx_n, dp_n = mesh.devices.shape
    devices = mesh.devices.reshape(8, ctx_n // 16, 2, dp_n // 4, 4)
    fine = Mesh(devices, CTX + DP)
    return jax.shard_map(
        body,
        mesh=fine,
        in_specs=(
            P(DP, CTX, None),
            P(DP, CTX, None),
            P(DP, CTX, None),
            P(DP, CTX, None),
            P(CTX, None),
            P(None, None, CTX),
            P(CTX, None),
        ),
        out_specs=(P(DP, CTX, None), P(CTX, None)),
        check_vma=False,
    )
```

```python
import jax
import jax.numpy as jnp
from jax import lax
from jax.sharding import Mesh
from jax.sharding import PartitionSpec as P

DILATION = 32

NOISE_SCALE = 0.1

CTX = ("y", "zl", "c")
DP = ("zh", "x")


def _size(axes):
    n = 1
    for a in axes:
        n *= lax.axis_size(a)
    return n


def _swap(x, axis, d):
    n = lax.axis_size(axis)
    return lax.ppermute(x, axis, [(i, i ^ d) for i in range(n)])


def _bit(axis, d):
    return (lax.axis_index(axis) // d) % 2


DIGITS = (("y", 4), ("y", 2), ("y", 1), ("zl", 2), ("zl", 1), ("c", 1))


def _gather_rows(piece, order):
    held = piece.reshape((1,) * len(DIGITS) + piece.shape)
    for axis, d in order:
        dim = DIGITS.index((axis, d))
        theirs = _swap(held, axis, d)
        low = jnp.concatenate([held, theirs], axis=dim)
        high = jnp.concatenate([theirs, held], axis=dim)
        held = jnp.where(_bit(axis, d) == 0, low, high)
    return held.reshape((-1,) + piece.shape[1:])


def _scatter_rows(full, order, shard):
    held = full.reshape((2,) * len(DIGITS) + (shard,) + full.shape[1:])
    for axis, d in order:
        dim = DIGITS.index((axis, d))
        mine = _bit(axis, d)
        keep = lax.dynamic_index_in_dim(held, mine, axis=dim, keepdims=True)
        give = lax.dynamic_index_in_dim(held, 1 - mine, axis=dim, keepdims=True)
        held = keep + _swap(give, axis, d)
    return held.reshape((shard,) + full.shape[1:])


def _sum_all(x, steps):
    for axis, d in steps:
        x = x + _swap(x, axis, d)
    return x


def body(features, bottleneck, node_noise, targets, entry_weight, conv_filters, exit_weight):
    feats = features[0]
    bottle = bottleneck[0]
    jitter = node_noise[0]
    goal = targets[0].astype(jnp.float32)
    rows, chans = feats.shape
    bot = bottle.shape[1]
    n_ctx = _size(CTX)
    ny, nz, nc = (lax.axis_size(a) for a in CTX)
    shard = entry_weight.shape[0]

    summed = lax.dot_general(
        bottle, jitter, (((0,), (0,)), ((), ())), preferred_element_type=jnp.float32
    )
    summed = _scatter_rows(
        summed, (("c", 1), ("zl", 1), ("zl", 2), ("y", 1), ("y", 2), ("y", 4)), shard
    )

    conv_rows = conv_filters.transpose(2, 0, 1).reshape(shard, -1)
    packed = jnp.concatenate([entry_weight, conv_rows, exit_weight], axis=1)
    for axis in ("y", "zl", "c"):
        packed = lax.all_gather(packed, axis, axis=0, tiled=True)
    w_entry = packed[:, :chans]
    w_conv = packed[:, chans : 4 * chans].reshape(bot, 3, chans)
    w_exit = packed[:, 4 * chans :]

    spacing = DILATION
    edge_in = jnp.concatenate([feats, bottle, jitter], axis=1)
    pairs_up = [(i, i + 1) for i in range(n_ctx - 1)]
    pairs_down = [(i + 1, i) for i in range(n_ctx - 1)]
    from_prev = lax.ppermute(edge_in[rows - spacing :], CTX, pairs_up)
    from_next = lax.ppermute(edge_in[:spacing], CTX, pairs_down)
    ext = jnp.concatenate([from_prev, edge_in, from_next], axis=0)
    ext_feats = ext[:, :chans]
    ny, nz, nc = (lax.axis_size(a) for a in CTX)
    ext_bottle = (
        ext[:, chans : chans + bot]
        .reshape(-1, ny, nz, nc, shard)
        .transpose(0, 3, 2, 1, 4)
        .reshape(-1, bot)
    )
    ext_jitter = ext[:, chans + bot :]

    baseline = ext_feats.astype(jnp.float32) + jnp.dot(
        ext_bottle, w_entry, preferred_element_type=jnp.float32
    )
    offset = ext_jitter.astype(jnp.float32) * NOISE_SCALE
    state = jnp.stack([baseline + offset, baseline - offset])
    activated = jax.nn.gelu(state).astype(jnp.bfloat16)
    mixed = None
    for k in range(3):
        term = lax.dot_general(
            activated[:, k * spacing : k * spacing + rows],
            w_conv[:, k, :],
            (((2,), (1,)), ((), ())),
            preferred_element_type=jnp.float32,
        )
        mixed = term if mixed is None else mixed + term
    inner = jax.nn.gelu(mixed).astype(jnp.bfloat16)
    outs = state[:, spacing : spacing + rows] + jnp.dot(
        inner, w_exit, preferred_element_type=jnp.float32
    )
    upper = outs[0]
    lower = outs[1]
    blended = ((upper + lower) * 0.5).astype(jnp.bfloat16)[None]
    local_gap = jnp.sum((upper - lower) * (upper + lower - 2.0 * goal)) / (rows * n_ctx * chans)
    gap = local_gap
    for axis in ("c", "zl", "y"):
        gap = lax.psum(gap, axis)
    factor = gap / (2.0 * NOISE_SCALE)
    estimate = _sum_all(factor * summed, (("x", 1), ("x", 2), ("zh", 1)))
    return (blended, estimate)


def solution(mesh):
    ctx_n, dp_n = mesh.devices.shape
    devices = mesh.devices.reshape(8, ctx_n // 16, 2, dp_n // 4, 4)
    fine = Mesh(devices, CTX + DP)
    return jax.shard_map(
        body,
        mesh=fine,
        in_specs=(
            P(DP, CTX, None),
            P(DP, CTX, None),
            P(DP, CTX, None),
            P(DP, CTX, None),
            P(CTX, None),
            P(None, None, CTX),
            P(CTX, None),
        ),
        out_specs=(P(DP, CTX, None), P(CTX, None)),
        check_vma=False,
    )
```

```python
import jax
import jax.numpy as jnp
from jax import lax
from jax.sharding import Mesh
from jax.sharding import PartitionSpec as P

DILATION = 32

NOISE_SCALE = 0.1

CTX = ("y", "zl", "c")
DP = ("zh", "x")


def _size(axes):
    n = 1
    for a in axes:
        n *= lax.axis_size(a)
    return n


def _swap(x, axis, d):
    n = lax.axis_size(axis)
    return lax.ppermute(x, axis, [(i, i ^ d) for i in range(n)])


def _bit(axis, d):
    return (lax.axis_index(axis) // d) % 2


DIGITS = (("y", 4), ("y", 2), ("y", 1), ("zl", 2), ("zl", 1), ("c", 1))


def _gather_rows(piece, order):
    held = piece.reshape((1,) * len(DIGITS) + piece.shape)
    for axis, d in order:
        dim = DIGITS.index((axis, d))
        theirs = _swap(held, axis, d)
        low = jnp.concatenate([held, theirs], axis=dim)
        high = jnp.concatenate([theirs, held], axis=dim)
        held = jnp.where(_bit(axis, d) == 0, low, high)
    return held.reshape((-1,) + piece.shape[1:])


def _scatter_rows(full, order, shard):
    held = full.reshape((2,) * len(DIGITS) + (shard,) + full.shape[1:])
    for axis, d in order:
        dim = DIGITS.index((axis, d))
        mine = _bit(axis, d)
        keep = lax.dynamic_index_in_dim(held, mine, axis=dim, keepdims=True)
        give = lax.dynamic_index_in_dim(held, 1 - mine, axis=dim, keepdims=True)
        held = keep + _swap(give, axis, d)
    return held.reshape((shard,) + full.shape[1:])


def _sum_all(x, steps):
    for axis, d in steps:
        x = x + _swap(x, axis, d)
    return x


def body(features, bottleneck, node_noise, targets, entry_weight, conv_filters, exit_weight):
    feats = features[0]
    bottle = bottleneck[0]
    jitter = node_noise[0]
    goal = targets[0].astype(jnp.float32)
    rows, chans = feats.shape
    bot = bottle.shape[1]
    n_ctx = _size(CTX)
    ny, nz, nc = (lax.axis_size(a) for a in CTX)
    shard = entry_weight.shape[0]

    summed = lax.dot_general(
        bottle, jitter, (((0,), (0,)), ((), ())), preferred_element_type=jnp.float32
    )

    conv_rows = conv_filters.transpose(2, 0, 1).reshape(shard, -1)
    packed = jnp.concatenate([entry_weight, conv_rows, exit_weight], axis=1)
    for axis in ("y", "zl", "c"):
        packed = lax.all_gather(packed, axis, axis=0, tiled=True)
    w_entry = packed[:, :chans]
    w_conv = packed[:, chans : 4 * chans].reshape(bot, 3, chans)
    w_exit = packed[:, 4 * chans :]

    spacing = DILATION
    edge_in = jnp.concatenate([feats, bottle, jitter], axis=1)
    pairs_up = [(i, i + 1) for i in range(n_ctx - 1)]
    pairs_down = [(i + 1, i) for i in range(n_ctx - 1)]
    from_prev = lax.ppermute(edge_in[rows - spacing :], CTX, pairs_up)
    from_next = lax.ppermute(edge_in[:spacing], CTX, pairs_down)
    ext = jnp.concatenate([from_prev, edge_in, from_next], axis=0)
    ext_feats = ext[:, :chans]
    ext_bottle = (
        ext[:, chans : chans + bot]
        .reshape(-1, ny, nz, nc, shard)
        .transpose(0, 3, 2, 1, 4)
        .reshape(-1, bot)
    )
    ext_jitter = ext[:, chans + bot :]

    baseline = ext_feats.astype(jnp.float32) + jnp.dot(
        ext_bottle, w_entry, preferred_element_type=jnp.float32
    )
    offset = ext_jitter.astype(jnp.float32) * NOISE_SCALE
    state = jnp.stack([baseline + offset, baseline - offset])
    activated = jax.nn.gelu(state).astype(jnp.bfloat16)
    mixed = None
    for k in range(3):
        term = lax.dot_general(
            activated[:, k * spacing : k * spacing + rows],
            w_conv[:, k, :],
            (((2,), (1,)), ((), ())),
            preferred_element_type=jnp.float32,
        )
        mixed = term if mixed is None else mixed + term
    inner = jax.nn.gelu(mixed).astype(jnp.bfloat16)
    outs = state[:, spacing : spacing + rows] + jnp.dot(
        inner, w_exit, preferred_element_type=jnp.float32
    )
    upper = outs[0]
    lower = outs[1]
    blended = ((upper + lower) * 0.5).astype(jnp.bfloat16)[None]
    local_gap = jnp.sum((upper - lower) * (upper + lower - 2.0 * goal)) / (rows * n_ctx * chans)
    lanes = 128
    with_gap = jnp.concatenate(
        [summed, jnp.broadcast_to(local_gap, (summed.shape[0], lanes))], axis=1
    )
    with_gap = _scatter_rows(
        with_gap, (("c", 1), ("zl", 1), ("zl", 2), ("y", 1), ("y", 2), ("y", 4)), shard
    )
    summed = with_gap[:, :chans]
    gap = with_gap[0, chans]
    factor = gap / (2.0 * NOISE_SCALE)
    estimate = _sum_all(factor * summed, (("x", 1), ("x", 2), ("zh", 1)))
    return (blended, estimate)


def solution(mesh):
    ctx_n, dp_n = mesh.devices.shape
    devices = mesh.devices.reshape(8, ctx_n // 16, 2, dp_n // 4, 4)
    fine = Mesh(devices, CTX + DP)
    return jax.shard_map(
        body,
        mesh=fine,
        in_specs=(
            P(DP, CTX, None),
            P(DP, CTX, None),
            P(DP, CTX, None),
            P(DP, CTX, None),
            P(CTX, None),
            P(None, None, CTX),
            P(CTX, None),
        ),
        out_specs=(P(DP, CTX, None), P(CTX, None)),
        check_vma=False,
    )
```

```python
import jax
import jax.numpy as jnp
from jax import lax
from jax.sharding import Mesh
from jax.sharding import PartitionSpec as P

DILATION = 32

NOISE_SCALE = 0.1

CTX = ("y", "zl", "c")
DP = ("zh", "x")


def _size(axes):
    n = 1
    for a in axes:
        n *= lax.axis_size(a)
    return n


def _swap(x, axis, d):
    n = lax.axis_size(axis)
    return lax.ppermute(x, axis, [(i, i ^ d) for i in range(n)])


def _bit(axis, d):
    return (lax.axis_index(axis) // d) % 2


DIGITS = (("y", 4), ("y", 2), ("y", 1), ("zl", 2), ("zl", 1), ("c", 1))


def _gather_rows(piece, order):
    held = piece.reshape((1,) * len(DIGITS) + piece.shape)
    for axis, d in order:
        dim = DIGITS.index((axis, d))
        theirs = _swap(held, axis, d)
        low = jnp.concatenate([held, theirs], axis=dim)
        high = jnp.concatenate([theirs, held], axis=dim)
        held = jnp.where(_bit(axis, d) == 0, low, high)
    return held.reshape((-1,) + piece.shape[1:])


def _scatter_rows(full, order, shard):
    held = full.reshape((2,) * len(DIGITS) + (shard,) + full.shape[1:])
    for axis, d in order:
        dim = DIGITS.index((axis, d))
        mine = _bit(axis, d)
        keep = lax.dynamic_index_in_dim(held, mine, axis=dim, keepdims=True)
        give = lax.dynamic_index_in_dim(held, 1 - mine, axis=dim, keepdims=True)
        held = keep + _swap(give, axis, d)
    return held.reshape((shard,) + full.shape[1:])


def _sum_all(x, steps):
    for axis, d in steps:
        x = x + _swap(x, axis, d)
    return x


def body(features, bottleneck, node_noise, targets, entry_weight, conv_filters, exit_weight):
    feats = features[0]
    bottle = bottleneck[0]
    jitter = node_noise[0]
    goal = targets[0].astype(jnp.float32)
    rows, chans = feats.shape
    bot = bottle.shape[1]
    n_ctx = _size(CTX)
    ny, nz, nc = (lax.axis_size(a) for a in CTX)
    shard = entry_weight.shape[0]

    summed = lax.dot_general(
        bottle, jitter, (((0,), (0,)), ((), ())), preferred_element_type=jnp.float32
    )
    summed = _scatter_rows(
        summed, (("c", 1), ("zl", 1), ("zl", 2), ("y", 1), ("y", 2), ("y", 4)), shard
    )

    conv_rows = conv_filters.transpose(2, 0, 1).reshape(shard, -1)
    packed = jnp.concatenate([entry_weight, conv_rows, exit_weight], axis=1)
    for axis in ("zl", "y", "c"):
        packed = lax.all_gather(packed, axis, axis=0, tiled=True)
    w_entry = packed[:, :chans]
    w_conv = packed[:, chans : 4 * chans].reshape(bot, 3, chans)
    w_exit = packed[:, 4 * chans :]

    spacing = DILATION
    edge_in = jnp.concatenate([feats, bottle, jitter], axis=1)
    pairs_up = [(i, i + 1) for i in range(n_ctx - 1)]
    pairs_down = [(i + 1, i) for i in range(n_ctx - 1)]
    from_prev = lax.ppermute(edge_in[rows - spacing :], CTX, pairs_up)
    from_next = lax.ppermute(edge_in[:spacing], CTX, pairs_down)
    ext = jnp.concatenate([from_prev, edge_in, from_next], axis=0)
    ext_feats = ext[:, :chans]
    ext_bottle = (
        ext[:, chans : chans + bot]
        .reshape(-1, ny, nz, nc, shard)
        .transpose(0, 3, 1, 2, 4)
        .reshape(-1, bot)
    )
    ext_jitter = ext[:, chans + bot :]

    baseline = ext_feats.astype(jnp.float32) + jnp.dot(
        ext_bottle, w_entry, preferred_element_type=jnp.float32
    )
    offset = ext_jitter.astype(jnp.float32) * NOISE_SCALE
    state = jnp.stack([baseline + offset, baseline - offset])
    activated = jax.nn.gelu(state).astype(jnp.bfloat16)
    mixed = None
    for k in range(3):
        term = lax.dot_general(
            activated[:, k * spacing : k * spacing + rows],
            w_conv[:, k, :],
            (((2,), (1,)), ((), ())),
            preferred_element_type=jnp.float32,
        )
        mixed = term if mixed is None else mixed + term
    inner = jax.nn.gelu(mixed).astype(jnp.bfloat16)
    outs = state[:, spacing : spacing + rows] + jnp.dot(
        inner, w_exit, preferred_element_type=jnp.float32
    )
    upper = outs[0]
    lower = outs[1]
    blended = ((upper + lower) * 0.5).astype(jnp.bfloat16)[None]
    local_gap = jnp.sum((upper - lower) * (upper + lower - 2.0 * goal)) / (rows * n_ctx * chans)
    gap = local_gap
    for axis in ("c", "zl", "y"):
        gap = lax.psum(gap, axis)
    factor = gap / (2.0 * NOISE_SCALE)
    estimate = _sum_all(factor * summed, (("x", 1), ("x", 2), ("zh", 1)))
    return (blended, estimate)


def solution(mesh):
    ctx_n, dp_n = mesh.devices.shape
    devices = mesh.devices.reshape(8, ctx_n // 16, 2, dp_n // 4, 4)
    fine = Mesh(devices, CTX + DP)
    return jax.shard_map(
        body,
        mesh=fine,
        in_specs=(
            P(DP, CTX, None),
            P(DP, CTX, None),
            P(DP, CTX, None),
            P(DP, CTX, None),
            P(CTX, None),
            P(None, None, CTX),
            P(CTX, None),
        ),
        out_specs=(P(DP, CTX, None), P(CTX, None)),
        check_vma=False,
    )
```

```python
import jax
import jax.numpy as jnp
from jax import lax
from jax.sharding import Mesh
from jax.sharding import PartitionSpec as P

DILATION = 32

NOISE_SCALE = 0.1

CTX = ("y", "zl", "c")
DP = ("zh", "x")


def _size(axes):
    n = 1
    for a in axes:
        n *= lax.axis_size(a)
    return n


def _swap(x, axis, d):
    n = lax.axis_size(axis)
    return lax.ppermute(x, axis, [(i, i ^ d) for i in range(n)])


def _bit(axis, d):
    return (lax.axis_index(axis) // d) % 2


DIGITS = (("y", 4), ("y", 2), ("y", 1), ("zl", 2), ("zl", 1), ("c", 1))


def _gather_rows(piece, order):
    held = piece.reshape((1,) * len(DIGITS) + piece.shape)
    for axis, d in order:
        dim = DIGITS.index((axis, d))
        theirs = _swap(held, axis, d)
        low = jnp.concatenate([held, theirs], axis=dim)
        high = jnp.concatenate([theirs, held], axis=dim)
        held = jnp.where(_bit(axis, d) == 0, low, high)
    return held.reshape((-1,) + piece.shape[1:])


def _scatter_rows(full, order, shard):
    held = full.reshape((2,) * len(DIGITS) + (shard,) + full.shape[1:])
    for axis, d in order:
        dim = DIGITS.index((axis, d))
        mine = _bit(axis, d)
        keep = lax.dynamic_index_in_dim(held, mine, axis=dim, keepdims=True)
        give = lax.dynamic_index_in_dim(held, 1 - mine, axis=dim, keepdims=True)
        held = keep + _swap(give, axis, d)
    return held.reshape((shard,) + full.shape[1:])


def _sum_all(x, steps):
    for axis, d in steps:
        x = x + _swap(x, axis, d)
    return x


def body(features, bottleneck, node_noise, targets, entry_weight, conv_filters, exit_weight):
    feats = features[0]
    bottle = bottleneck[0]
    jitter = node_noise[0]
    goal = targets[0].astype(jnp.float32)
    rows, chans = feats.shape
    bot = bottle.shape[1]
    n_ctx = _size(CTX)
    ny, nz, nc = (lax.axis_size(a) for a in CTX)
    shard = entry_weight.shape[0]

    summed = lax.dot_general(
        bottle, jitter, (((0,), (0,)), ((), ())), preferred_element_type=jnp.float32
    )

    conv_rows = conv_filters.transpose(2, 0, 1).reshape(shard, -1)
    packed = jnp.concatenate([entry_weight, conv_rows, exit_weight], axis=1)
    for axis in ("zl", "y"):
        packed = lax.all_gather(packed, axis, axis=0, tiled=True)
    summed = _scatter_rows(
        summed, (("c", 1), ("zl", 1), ("zl", 2), ("y", 1), ("y", 2), ("y", 4)), shard
    )
    packed, summed = lax.optimization_barrier((packed, summed))
    packed = lax.all_gather(packed, "c", axis=0, tiled=True)
    w_entry = packed[:, :chans]
    w_conv = packed[:, chans : 4 * chans].reshape(bot, 3, chans)
    w_exit = packed[:, 4 * chans :]

    spacing = DILATION
    edge_in = jnp.concatenate([feats, bottle, jitter], axis=1)
    pairs_up = [(i, i + 1) for i in range(n_ctx - 1)]
    pairs_down = [(i + 1, i) for i in range(n_ctx - 1)]
    from_prev = lax.ppermute(edge_in[rows - spacing :], CTX, pairs_up)
    from_next = lax.ppermute(edge_in[:spacing], CTX, pairs_down)
    ext = jnp.concatenate([from_prev, edge_in, from_next], axis=0)
    ext_feats = ext[:, :chans]
    ext_bottle = (
        ext[:, chans : chans + bot]
        .reshape(-1, ny, nz, nc, shard)
        .transpose(0, 3, 1, 2, 4)
        .reshape(-1, bot)
    )
    ext_jitter = ext[:, chans + bot :]

    baseline = ext_feats.astype(jnp.float32) + jnp.dot(
        ext_bottle, w_entry, preferred_element_type=jnp.float32
    )
    offset = ext_jitter.astype(jnp.float32) * NOISE_SCALE
    state = jnp.stack([baseline + offset, baseline - offset])
    activated = jax.nn.gelu(state).astype(jnp.bfloat16)
    mixed = None
    for k in range(3):
        term = lax.dot_general(
            activated[:, k * spacing : k * spacing + rows],
            w_conv[:, k, :],
            (((2,), (1,)), ((), ())),
            preferred_element_type=jnp.float32,
        )
        mixed = term if mixed is None else mixed + term
    inner = jax.nn.gelu(mixed).astype(jnp.bfloat16)
    outs = state[:, spacing : spacing + rows] + jnp.dot(
        inner, w_exit, preferred_element_type=jnp.float32
    )
    upper = outs[0]
    lower = outs[1]
    blended = ((upper + lower) * 0.5).astype(jnp.bfloat16)[None]
    local_gap = jnp.sum((upper - lower) * (upper + lower - 2.0 * goal)) / (rows * n_ctx * chans)
    gap = local_gap
    for axis in ("c", "zl", "y"):
        gap = lax.psum(gap, axis)
    factor = gap / (2.0 * NOISE_SCALE)
    estimate = _sum_all(factor * summed, (("x", 1), ("x", 2), ("zh", 1)))
    return (blended, estimate)


def solution(mesh):
    ctx_n, dp_n = mesh.devices.shape
    devices = mesh.devices.reshape(8, ctx_n // 16, 2, dp_n // 4, 4)
    fine = Mesh(devices, CTX + DP)
    return jax.shard_map(
        body,
        mesh=fine,
        in_specs=(
            P(DP, CTX, None),
            P(DP, CTX, None),
            P(DP, CTX, None),
            P(DP, CTX, None),
            P(CTX, None),
            P(None, None, CTX),
            P(CTX, None),
        ),
        out_specs=(P(DP, CTX, None), P(CTX, None)),
        check_vma=False,
    )
```

```python
import jax
import jax.numpy as jnp
from jax import lax
from jax.sharding import Mesh
from jax.sharding import PartitionSpec as P

DILATION = 32

NOISE_SCALE = 0.1

CTX = ("y", "zl", "c")
DP = ("zh", "x")


def _size(axes):
    n = 1
    for a in axes:
        n *= lax.axis_size(a)
    return n


def _swap(x, axis, d):
    n = lax.axis_size(axis)
    return lax.ppermute(x, axis, [(i, i ^ d) for i in range(n)])


def _bit(axis, d):
    return (lax.axis_index(axis) // d) % 2


DIGITS = (("y", 4), ("y", 2), ("y", 1), ("zl", 2), ("zl", 1), ("c", 1))


def _gather_rows(piece, order):
    held = piece.reshape((1,) * len(DIGITS) + piece.shape)
    for axis, d in order:
        dim = DIGITS.index((axis, d))
        theirs = _swap(held, axis, d)
        low = jnp.concatenate([held, theirs], axis=dim)
        high = jnp.concatenate([theirs, held], axis=dim)
        held = jnp.where(_bit(axis, d) == 0, low, high)
    return held.reshape((-1,) + piece.shape[1:])


def _scatter_rows(full, order, shard):
    held = full.reshape((2,) * len(DIGITS) + (shard,) + full.shape[1:])
    for axis, d in order:
        dim = DIGITS.index((axis, d))
        mine = _bit(axis, d)
        keep = lax.dynamic_index_in_dim(held, mine, axis=dim, keepdims=True)
        give = lax.dynamic_index_in_dim(held, 1 - mine, axis=dim, keepdims=True)
        held = keep + _swap(give.astype(jnp.bfloat16), axis, d).astype(full.dtype)
    return held.reshape((shard,) + full.shape[1:])


def _sum_all(x, steps):
    for axis, d in steps:
        x = x + _swap(x, axis, d)
    return x


def body(features, bottleneck, node_noise, targets, entry_weight, conv_filters, exit_weight):
    feats = features[0]
    bottle = bottleneck[0]
    jitter = node_noise[0]
    goal = targets[0].astype(jnp.float32)
    rows, chans = feats.shape
    bot = bottle.shape[1]
    n_ctx = _size(CTX)
    ny, nz, nc = (lax.axis_size(a) for a in CTX)
    shard = entry_weight.shape[0]

    summed = lax.dot_general(
        bottle, jitter, (((0,), (0,)), ((), ())), preferred_element_type=jnp.float32
    )

    conv_rows = conv_filters.transpose(2, 0, 1).reshape(shard, -1)
    packed = jnp.concatenate([entry_weight, conv_rows, exit_weight], axis=1)
    for axis in ("zl", "y"):
        packed = lax.all_gather(packed, axis, axis=0, tiled=True)
    summed = _scatter_rows(
        summed, (("c", 1), ("zl", 1), ("zl", 2), ("y", 1), ("y", 2), ("y", 4)), shard
    )
    packed, summed = lax.optimization_barrier((packed, summed))
    packed = lax.all_gather(packed, "c", axis=0, tiled=True)
    w_entry = packed[:, :chans]
    w_conv = packed[:, chans : 4 * chans].reshape(bot, 3, chans)
    w_exit = packed[:, 4 * chans :]

    spacing = DILATION
    edge_in = jnp.concatenate([feats, bottle, jitter], axis=1)
    pairs_up = [(i, i + 1) for i in range(n_ctx - 1)]
    pairs_down = [(i + 1, i) for i in range(n_ctx - 1)]
    from_prev = lax.ppermute(edge_in[rows - spacing :], CTX, pairs_up)
    from_next = lax.ppermute(edge_in[:spacing], CTX, pairs_down)
    ext = jnp.concatenate([from_prev, edge_in, from_next], axis=0)
    ext_feats = ext[:, :chans]
    ext_bottle = (
        ext[:, chans : chans + bot]
        .reshape(-1, ny, nz, nc, shard)
        .transpose(0, 3, 1, 2, 4)
        .reshape(-1, bot)
    )
    ext_jitter = ext[:, chans + bot :]

    baseline = ext_feats.astype(jnp.float32) + jnp.dot(
        ext_bottle, w_entry, preferred_element_type=jnp.float32
    )
    offset = ext_jitter.astype(jnp.float32) * NOISE_SCALE
    state = jnp.stack([baseline + offset, baseline - offset])
    activated = jax.nn.gelu(state).astype(jnp.bfloat16)
    mixed = None
    for k in range(3):
        term = lax.dot_general(
            activated[:, k * spacing : k * spacing + rows],
            w_conv[:, k, :],
            (((2,), (1,)), ((), ())),
            preferred_element_type=jnp.float32,
        )
        mixed = term if mixed is None else mixed + term
    inner = jax.nn.gelu(mixed).astype(jnp.bfloat16)
    outs = state[:, spacing : spacing + rows] + jnp.dot(
        inner, w_exit, preferred_element_type=jnp.float32
    )
    upper = outs[0]
    lower = outs[1]
    blended = ((upper + lower) * 0.5).astype(jnp.bfloat16)[None]
    local_gap = jnp.sum((upper - lower) * (upper + lower - 2.0 * goal)) / (rows * n_ctx * chans)
    gap = local_gap
    for axis in ("c", "zl", "y"):
        gap = lax.psum(gap, axis)
    factor = gap / (2.0 * NOISE_SCALE)
    estimate = _sum_all(factor * summed, (("x", 1), ("x", 2), ("zh", 1)))
    return (blended, estimate)


def solution(mesh):
    ctx_n, dp_n = mesh.devices.shape
    devices = mesh.devices.reshape(8, ctx_n // 16, 2, dp_n // 4, 4)
    fine = Mesh(devices, CTX + DP)
    return jax.shard_map(
        body,
        mesh=fine,
        in_specs=(
            P(DP, CTX, None),
            P(DP, CTX, None),
            P(DP, CTX, None),
            P(DP, CTX, None),
            P(CTX, None),
            P(None, None, CTX),
            P(CTX, None),
        ),
        out_specs=(P(DP, CTX, None), P(CTX, None)),
        check_vma=False,
    )
```

```python
import jax
import jax.numpy as jnp
from jax import lax
from jax.sharding import Mesh
from jax.sharding import PartitionSpec as P

DILATION = 32

NOISE_SCALE = 0.1

CTX = ("y", "zl", "c")
DP = ("zh", "x")


def _size(axes):
    n = 1
    for a in axes:
        n *= lax.axis_size(a)
    return n


def _swap(x, axis, d):
    n = lax.axis_size(axis)
    return lax.ppermute(x, axis, [(i, i ^ d) for i in range(n)])


def _bit(axis, d):
    return (lax.axis_index(axis) // d) % 2


DIGITS = (("y", 4), ("y", 2), ("y", 1), ("zl", 2), ("zl", 1), ("c", 1))


def _gather_rows(piece, order):
    held = piece.reshape((1,) * len(DIGITS) + piece.shape)
    for axis, d in order:
        dim = DIGITS.index((axis, d))
        theirs = _swap(held, axis, d)
        low = jnp.concatenate([held, theirs], axis=dim)
        high = jnp.concatenate([theirs, held], axis=dim)
        held = jnp.where(_bit(axis, d) == 0, low, high)
    return held.reshape((-1,) + piece.shape[1:])


def _halve(held, order):
    for axis, d in order:
        dim = DIGITS.index((axis, d))
        mine = _bit(axis, d)
        keep = lax.dynamic_index_in_dim(held, mine, axis=dim, keepdims=True)
        give = lax.dynamic_index_in_dim(held, 1 - mine, axis=dim, keepdims=True)
        held = keep + _swap(give.astype(jnp.bfloat16), axis, d).astype(held.dtype)
    return held


def _sum_all(x, steps):
    for axis, d in steps:
        x = x + _swap(x, axis, d)
    return x


def body(features, bottleneck, node_noise, targets, entry_weight, conv_filters, exit_weight):
    feats = features[0]
    bottle = bottleneck[0]
    jitter = node_noise[0]
    goal = targets[0].astype(jnp.float32)
    rows, chans = feats.shape
    bot = bottle.shape[1]
    n_ctx = _size(CTX)
    ny, nz, nc = (lax.axis_size(a) for a in CTX)
    shard = entry_weight.shape[0]

    summed = lax.dot_general(
        bottle, jitter, (((0,), (0,)), ((), ())), preferred_element_type=jnp.float32
    )

    conv_rows = conv_filters.transpose(2, 0, 1).reshape(shard, -1)
    packed = jnp.concatenate([entry_weight, conv_rows, exit_weight], axis=1)
    for axis in ("zl", "y"):
        packed = lax.all_gather(packed, axis, axis=0, tiled=True)

    spacing = DILATION
    edge_in = jnp.concatenate([feats, bottle, jitter], axis=1)
    pairs_up = [(i, i + 1) for i in range(n_ctx - 1)]
    pairs_down = [(i + 1, i) for i in range(n_ctx - 1)]
    from_prev = lax.ppermute(edge_in[rows - spacing :], CTX, pairs_up)
    from_next = lax.ppermute(edge_in[:spacing], CTX, pairs_down)

    summed = summed.reshape((2,) * len(DIGITS) + (shard, chans))
    summed = _halve(summed, (("c", 1), ("zl", 1), ("zl", 2)))
    packed, summed, from_prev, from_next = lax.optimization_barrier(
        (packed, summed, from_prev, from_next)
    )
    packed = lax.all_gather(packed, "c", axis=0, tiled=True)
    summed = _halve(summed, (("y", 1), ("y", 2), ("y", 4)))
    packed, summed = lax.optimization_barrier((packed, summed))
    summed = summed.reshape(shard, chans)
    w_entry = packed[:, :chans]
    w_conv = packed[:, chans : 4 * chans].reshape(bot, 3, chans)
    w_exit = packed[:, 4 * chans :]

    ext = jnp.concatenate([from_prev, edge_in, from_next], axis=0)
    ext_feats = ext[:, :chans]
    ext_bottle = (
        ext[:, chans : chans + bot]
        .reshape(-1, ny, nz, nc, shard)
        .transpose(0, 3, 1, 2, 4)
        .reshape(-1, bot)
    )
    ext_jitter = ext[:, chans + bot :]

    baseline = ext_feats.astype(jnp.float32) + jnp.dot(
        ext_bottle, w_entry, preferred_element_type=jnp.float32
    )
    offset = ext_jitter.astype(jnp.float32) * NOISE_SCALE
    state = jnp.stack([baseline + offset, baseline - offset])
    activated = jax.nn.gelu(state).astype(jnp.bfloat16)
    mixed = None
    for k in range(3):
        term = lax.dot_general(
            activated[:, k * spacing : k * spacing + rows],
            w_conv[:, k, :],
            (((2,), (1,)), ((), ())),
            preferred_element_type=jnp.float32,
        )
        mixed = term if mixed is None else mixed + term
    inner = jax.nn.gelu(mixed).astype(jnp.bfloat16)
    outs = state[:, spacing : spacing + rows] + jnp.dot(
        inner, w_exit, preferred_element_type=jnp.float32
    )
    upper = outs[0]
    lower = outs[1]
    blended = ((upper + lower) * 0.5).astype(jnp.bfloat16)[None]
    local_gap = jnp.sum((upper - lower) * (upper + lower - 2.0 * goal)) / (rows * n_ctx * chans)
    gap = local_gap
    for axis in ("c", "zl", "y"):
        gap = lax.psum(gap, axis)
    factor = gap / (2.0 * NOISE_SCALE)
    estimate = _sum_all(factor * summed, (("x", 1), ("x", 2), ("zh", 1)))
    return (blended, estimate)


def solution(mesh):
    ctx_n, dp_n = mesh.devices.shape
    devices = mesh.devices.reshape(8, ctx_n // 16, 2, dp_n // 4, 4)
    fine = Mesh(devices, CTX + DP)
    return jax.shard_map(
        body,
        mesh=fine,
        in_specs=(
            P(DP, CTX, None),
            P(DP, CTX, None),
            P(DP, CTX, None),
            P(DP, CTX, None),
            P(CTX, None),
            P(None, None, CTX),
            P(CTX, None),
        ),
        out_specs=(P(DP, CTX, None), P(CTX, None)),
        check_vma=False,
    )
```

```python
import jax
import jax.numpy as jnp
from jax import lax
from jax.sharding import Mesh
from jax.sharding import PartitionSpec as P

DILATION = 32

NOISE_SCALE = 0.1

CTX = ("y", "zl", "c")
DP = ("zh", "x")


def _size(axes):
    n = 1
    for a in axes:
        n *= lax.axis_size(a)
    return n


def _swap(x, axis, d):
    n = lax.axis_size(axis)
    return lax.ppermute(x, axis, [(i, i ^ d) for i in range(n)])


def _bit(axis, d):
    return (lax.axis_index(axis) // d) % 2


DIGITS = (("y", 4), ("y", 2), ("y", 1), ("zl", 2), ("zl", 1), ("c", 1))


def _gather_rows(piece, order):
    held = piece.reshape((1,) * len(DIGITS) + piece.shape)
    for axis, d in order:
        dim = DIGITS.index((axis, d))
        theirs = _swap(held, axis, d)
        low = jnp.concatenate([held, theirs], axis=dim)
        high = jnp.concatenate([theirs, held], axis=dim)
        held = jnp.where(_bit(axis, d) == 0, low, high)
    return held.reshape((-1,) + piece.shape[1:])


def _halve(held, order):
    for axis, d in order:
        dim = DIGITS.index((axis, d))
        mine = _bit(axis, d)
        keep = lax.dynamic_index_in_dim(held, mine, axis=dim, keepdims=True)
        give = lax.dynamic_index_in_dim(held, 1 - mine, axis=dim, keepdims=True)
        held = keep + _swap(give.astype(jnp.bfloat16), axis, d).astype(held.dtype)
    return held


def _sum_all(x, steps):
    for axis, d in steps:
        x = x + _swap(x, axis, d)
    return x


def _sum_group(x, axes):
    n = _size(axes)
    vals = [x] + [lax.ppermute(x, axes, [(i, i ^ k) for i in range(n)]) for k in range(1, n)]
    while len(vals) > 1:
        vals = [vals[i] + vals[i + 1] for i in range(0, len(vals), 2)]
    return vals[0]


def body(features, bottleneck, node_noise, targets, entry_weight, conv_filters, exit_weight):
    feats = features[0]
    bottle = bottleneck[0]
    jitter = node_noise[0]
    goal = targets[0].astype(jnp.float32)
    rows, chans = feats.shape
    bot = bottle.shape[1]
    n_ctx = _size(CTX)
    ny, nz, nc = (lax.axis_size(a) for a in CTX)
    shard = entry_weight.shape[0]

    summed = lax.dot_general(
        bottle, jitter, (((0,), (0,)), ((), ())), preferred_element_type=jnp.float32
    )

    conv_rows = conv_filters.transpose(2, 0, 1).reshape(shard, -1)
    packed = jnp.concatenate([entry_weight, conv_rows, exit_weight], axis=1)
    for axis in ("zl", "y"):
        packed = lax.all_gather(packed, axis, axis=0, tiled=True)

    spacing = DILATION
    edge_in = jnp.concatenate([feats, bottle, jitter], axis=1)
    pairs_up = [(i, i + 1) for i in range(n_ctx - 1)]
    pairs_down = [(i + 1, i) for i in range(n_ctx - 1)]
    from_prev = lax.ppermute(edge_in[rows - spacing :], CTX, pairs_up)
    from_next = lax.ppermute(edge_in[:spacing], CTX, pairs_down)

    summed = summed.reshape((2,) * len(DIGITS) + (shard, chans))
    summed = _halve(summed, (("c", 1), ("zl", 1), ("zl", 2)))
    packed, summed, from_prev, from_next = lax.optimization_barrier(
        (packed, summed, from_prev, from_next)
    )
    packed = lax.all_gather(packed, "c", axis=0, tiled=True)
    summed = _halve(summed, (("y", 1), ("y", 2), ("y", 4)))
    packed, summed = lax.optimization_barrier((packed, summed))
    summed = summed.reshape(shard, chans)
    w_entry = packed[:, :chans]
    w_conv = packed[:, chans : 4 * chans].reshape(bot, 3, chans)
    w_exit = packed[:, 4 * chans :]

    ext = jnp.concatenate([from_prev, edge_in, from_next], axis=0)
    ext_feats = ext[:, :chans]
    ext_bottle = (
        ext[:, chans : chans + bot]
        .reshape(-1, ny, nz, nc, shard)
        .transpose(0, 3, 1, 2, 4)
        .reshape(-1, bot)
    )
    ext_jitter = ext[:, chans + bot :]

    baseline = ext_feats.astype(jnp.float32) + jnp.dot(
        ext_bottle, w_entry, preferred_element_type=jnp.float32
    )
    offset = ext_jitter.astype(jnp.float32) * NOISE_SCALE
    state = jnp.stack([baseline + offset, baseline - offset])
    activated = jax.nn.gelu(state).astype(jnp.bfloat16)
    mixed = None
    for k in range(3):
        term = lax.dot_general(
            activated[:, k * spacing : k * spacing + rows],
            w_conv[:, k, :],
            (((2,), (1,)), ((), ())),
            preferred_element_type=jnp.float32,
        )
        mixed = term if mixed is None else mixed + term
    inner = jax.nn.gelu(mixed).astype(jnp.bfloat16)
    outs = state[:, spacing : spacing + rows] + jnp.dot(
        inner, w_exit, preferred_element_type=jnp.float32
    )
    upper = outs[0]
    lower = outs[1]
    blended = ((upper + lower) * 0.5).astype(jnp.bfloat16)[None]
    local_gap = jnp.sum((upper - lower) * (upper + lower - 2.0 * goal)) / (rows * n_ctx * chans)
    gap = _sum_group(_sum_group(local_gap.reshape(1), ("zl", "c")), ("y",))
    factor = gap / (2.0 * NOISE_SCALE)
    estimate = _sum_group(factor * summed, DP)
    return (blended, estimate)


def solution(mesh):
    ctx_n, dp_n = mesh.devices.shape
    devices = mesh.devices.reshape(8, ctx_n // 16, 2, dp_n // 4, 4)
    fine = Mesh(devices, CTX + DP)
    return jax.shard_map(
        body,
        mesh=fine,
        in_specs=(
            P(DP, CTX, None),
            P(DP, CTX, None),
            P(DP, CTX, None),
            P(DP, CTX, None),
            P(CTX, None),
            P(None, None, CTX),
            P(CTX, None),
        ),
        out_specs=(P(DP, CTX, None), P(CTX, None)),
        check_vma=False,
    )
```

```python
import jax
import jax.numpy as jnp
from jax import lax
from jax.sharding import Mesh
from jax.sharding import PartitionSpec as P

DILATION = 32

NOISE_SCALE = 0.1

CTX = ("y", "zl", "c")
DP = ("zh", "x")


def _size(axes):
    n = 1
    for a in axes:
        n *= lax.axis_size(a)
    return n


def _swap(x, axis, d):
    n = lax.axis_size(axis)
    return lax.ppermute(x, axis, [(i, i ^ d) for i in range(n)])


def _bit(axis, d):
    return (lax.axis_index(axis) // d) % 2


DIGITS = (("y", 4), ("y", 2), ("y", 1), ("zl", 2), ("zl", 1), ("c", 1))


def _gather_rows(piece, order):
    held = piece.reshape((1,) * len(DIGITS) + piece.shape)
    for axis, d in order:
        dim = DIGITS.index((axis, d))
        theirs = _swap(held, axis, d)
        low = jnp.concatenate([held, theirs], axis=dim)
        high = jnp.concatenate([theirs, held], axis=dim)
        held = jnp.where(_bit(axis, d) == 0, low, high)
    return held.reshape((-1,) + piece.shape[1:])


def _halve(held, order):
    for axis, d in order:
        dim = DIGITS.index((axis, d))
        mine = _bit(axis, d)
        keep = lax.dynamic_index_in_dim(held, mine, axis=dim, keepdims=True)
        give = lax.dynamic_index_in_dim(held, 1 - mine, axis=dim, keepdims=True)
        held = keep + _swap(give.astype(jnp.bfloat16), axis, d).astype(held.dtype)
    return held


def _sum_all(x, steps):
    for axis, d in steps:
        x = x + _swap(x, axis, d)
    return x


def body(features, bottleneck, node_noise, targets, entry_weight, conv_filters, exit_weight):
    feats = features[0]
    bottle = bottleneck[0]
    jitter = node_noise[0]
    goal = targets[0].astype(jnp.float32)
    rows, chans = feats.shape
    bot = bottle.shape[1]
    n_ctx = _size(CTX)
    ny, nz, nc = (lax.axis_size(a) for a in CTX)
    shard = entry_weight.shape[0]

    summed = lax.dot_general(
        bottle, jitter, (((0,), (0,)), ((), ())), preferred_element_type=jnp.float32
    )

    conv_rows = conv_filters.transpose(2, 0, 1).reshape(shard, -1)
    packed = jnp.concatenate([entry_weight, conv_rows, exit_weight], axis=1)
    packed = lax.all_gather(packed, "zl", axis=0, tiled=True)
    half = packed.shape[1] // 2
    halves = [packed[:, :half], packed[:, half:]]
    halves = [lax.all_gather(h, "y", axis=0, tiled=True) for h in halves]

    spacing = DILATION
    edge_in = jnp.concatenate([feats, bottle, jitter], axis=1)
    pairs_up = [(i, i + 1) for i in range(n_ctx - 1)]
    pairs_down = [(i + 1, i) for i in range(n_ctx - 1)]
    from_prev = lax.ppermute(edge_in[rows - spacing :], CTX, pairs_up)
    from_next = lax.ppermute(edge_in[:spacing], CTX, pairs_down)

    summed = summed.reshape((2,) * len(DIGITS) + (shard, chans))
    summed = _halve(summed, (("c", 1), ("zl", 1), ("zl", 2)))
    halves, summed, from_prev, from_next = lax.optimization_barrier(
        (halves, summed, from_prev, from_next)
    )
    halves = [lax.all_gather(h, "c", axis=0, tiled=True) for h in halves]
    summed = _halve(summed, (("y", 1), ("y", 2), ("y", 4)))
    halves, summed = lax.optimization_barrier((halves, summed))
    summed = summed.reshape(shard, chans)
    first, second = halves
    w_entry = first[:, :chans]
    w_conv = jnp.concatenate([first[:, chans:], second[:, : 3 * chans - (half - chans)]], axis=1)
    w_conv = w_conv.reshape(bot, 3, chans)
    w_exit = second[:, 3 * chans - (half - chans) :]

    ext = jnp.concatenate([from_prev, edge_in, from_next], axis=0)
    ext_feats = ext[:, :chans]
    ext_bottle = (
        ext[:, chans : chans + bot]
        .reshape(-1, ny, nz, nc, shard)
        .transpose(0, 3, 1, 2, 4)
        .reshape(-1, bot)
    )
    ext_jitter = ext[:, chans + bot :]

    baseline = ext_feats.astype(jnp.float32) + jnp.dot(
        ext_bottle, w_entry, preferred_element_type=jnp.float32
    )
    offset = ext_jitter.astype(jnp.float32) * NOISE_SCALE
    state = jnp.stack([baseline + offset, baseline - offset])
    activated = jax.nn.gelu(state).astype(jnp.bfloat16)
    mixed = None
    for k in range(3):
        term = lax.dot_general(
            activated[:, k * spacing : k * spacing + rows],
            w_conv[:, k, :],
            (((2,), (1,)), ((), ())),
            preferred_element_type=jnp.float32,
        )
        mixed = term if mixed is None else mixed + term
    inner = jax.nn.gelu(mixed).astype(jnp.bfloat16)
    outs = state[:, spacing : spacing + rows] + jnp.dot(
        inner, w_exit, preferred_element_type=jnp.float32
    )
    upper = outs[0]
    lower = outs[1]
    blended = ((upper + lower) * 0.5).astype(jnp.bfloat16)[None]
    local_gap = jnp.sum((upper - lower) * (upper + lower - 2.0 * goal)) / (rows * n_ctx * chans)
    gap = local_gap
    for axis in ("c", "zl", "y"):
        gap = lax.psum(gap, axis)
    factor = gap / (2.0 * NOISE_SCALE)
    estimate = _sum_all(factor * summed, (("x", 1), ("x", 2), ("zh", 1)))
    return (blended, estimate)


def solution(mesh):
    ctx_n, dp_n = mesh.devices.shape
    devices = mesh.devices.reshape(8, ctx_n // 16, 2, dp_n // 4, 4)
    fine = Mesh(devices, CTX + DP)
    return jax.shard_map(
        body,
        mesh=fine,
        in_specs=(
            P(DP, CTX, None),
            P(DP, CTX, None),
            P(DP, CTX, None),
            P(DP, CTX, None),
            P(CTX, None),
            P(None, None, CTX),
            P(CTX, None),
        ),
        out_specs=(P(DP, CTX, None), P(CTX, None)),
        check_vma=False,
    )
```

```python
import jax
import jax.numpy as jnp
from jax import lax
from jax.sharding import Mesh
from jax.sharding import PartitionSpec as P

DILATION = 32

NOISE_SCALE = 0.1

CTX = ("y", "zl", "c")
DP = ("zh", "x")


def _size(axes):
    n = 1
    for a in axes:
        n *= lax.axis_size(a)
    return n


def _swap(x, axis, d):
    n = lax.axis_size(axis)
    return lax.ppermute(x, axis, [(i, i ^ d) for i in range(n)])


def _bit(axis, d):
    return (lax.axis_index(axis) // d) % 2


DIGITS = (("y", 4), ("y", 2), ("y", 1), ("zl", 2), ("zl", 1), ("c", 1))


def _gather_rows(piece, order):
    held = piece.reshape((1,) * len(DIGITS) + piece.shape)
    for axis, d in order:
        dim = DIGITS.index((axis, d))
        theirs = _swap(held, axis, d)
        low = jnp.concatenate([held, theirs], axis=dim)
        high = jnp.concatenate([theirs, held], axis=dim)
        held = jnp.where(_bit(axis, d) == 0, low, high)
    return held.reshape((-1,) + piece.shape[1:])


def _halve(held, order):
    for axis, d in order:
        dim = DIGITS.index((axis, d))
        mine = _bit(axis, d)
        keep = lax.dynamic_index_in_dim(held, mine, axis=dim, keepdims=True)
        give = lax.dynamic_index_in_dim(held, 1 - mine, axis=dim, keepdims=True)
        held = keep + _swap(give.astype(jnp.bfloat16), axis, d).astype(held.dtype)
    return held


def _sum_all(x, steps):
    for axis, d in steps:
        x = x + _swap(x, axis, d)
    return x


def body(features, bottleneck, node_noise, targets, entry_weight, conv_filters, exit_weight):
    feats = features[0]
    bottle = bottleneck[0]
    jitter = node_noise[0]
    goal = targets[0].astype(jnp.float32)
    rows, chans = feats.shape
    bot = bottle.shape[1]
    n_ctx = _size(CTX)
    ny, nz, nc = (lax.axis_size(a) for a in CTX)
    shard = entry_weight.shape[0]

    summed = lax.dot_general(
        bottle, jitter, (((0,), (0,)), ((), ())), preferred_element_type=jnp.float32
    )

    conv_rows = conv_filters.transpose(2, 0, 1).reshape(shard, -1)
    packed = jnp.concatenate([entry_weight, conv_rows, exit_weight], axis=1)
    for axis in ("zl", "y"):
        packed = lax.all_gather(packed, axis, axis=0, tiled=True)

    spacing = DILATION
    edge_in = jnp.concatenate([feats, bottle, jitter], axis=1)
    pairs_up = [(i, i + 1) for i in range(n_ctx - 1)]
    pairs_down = [(i + 1, i) for i in range(n_ctx - 1)]
    from_prev = lax.ppermute(edge_in[rows - spacing :], CTX, pairs_up)
    from_next = lax.ppermute(edge_in[:spacing], CTX, pairs_down)

    summed = summed.reshape((2,) * len(DIGITS) + (shard, chans))
    summed = _halve(summed, (("c", 1), ("zl", 1), ("zl", 2)))
    packed, summed, from_prev, from_next = lax.optimization_barrier(
        (packed, summed, from_prev, from_next)
    )
    theirs = _swap(packed, "c", 1)
    summed = _halve(summed, (("y", 1), ("y", 2), ("y", 4)))
    theirs, summed = lax.optimization_barrier((theirs, summed))
    packed = jnp.concatenate([packed, theirs], axis=0)
    summed = summed.reshape(shard, chans)
    w_entry = packed[:, :chans]
    w_conv = packed[:, chans : 4 * chans].reshape(bot, 3, chans)
    w_exit = packed[:, 4 * chans :]

    ext = jnp.concatenate([from_prev, edge_in, from_next], axis=0)
    ext_feats = ext[:, :chans]
    ext_bottle = ext[:, chans : chans + bot].reshape(-1, ny, nz, nc, shard).transpose(0, 3, 1, 2, 4)
    ext_bottle = jnp.where(lax.axis_index("c") == 0, ext_bottle, ext_bottle[:, ::-1]).reshape(-1, bot)
    ext_jitter = ext[:, chans + bot :]

    baseline = ext_feats.astype(jnp.float32) + jnp.dot(
        ext_bottle, w_entry, preferred_element_type=jnp.float32
    )
    offset = ext_jitter.astype(jnp.float32) * NOISE_SCALE
    state = jnp.stack([baseline + offset, baseline - offset])
    activated = jax.nn.gelu(state).astype(jnp.bfloat16)
    mixed = None
    for k in range(3):
        term = lax.dot_general(
            activated[:, k * spacing : k * spacing + rows],
            w_conv[:, k, :],
            (((2,), (1,)), ((), ())),
            preferred_element_type=jnp.float32,
        )
        mixed = term if mixed is None else mixed + term
    inner = jax.nn.gelu(mixed).astype(jnp.bfloat16)
    outs = state[:, spacing : spacing + rows] + jnp.dot(
        inner, w_exit, preferred_element_type=jnp.float32
    )
    upper = outs[0]
    lower = outs[1]
    blended = ((upper + lower) * 0.5).astype(jnp.bfloat16)[None]
    local_gap = jnp.sum((upper - lower) * (upper + lower - 2.0 * goal)) / (rows * n_ctx * chans)
    gap = local_gap
    for axis in ("c", "zl", "y"):
        gap = lax.psum(gap, axis)
    factor = gap / (2.0 * NOISE_SCALE)
    estimate = _sum_all(factor * summed, (("x", 1), ("x", 2), ("zh", 1)))
    return (blended, estimate)


def solution(mesh):
    ctx_n, dp_n = mesh.devices.shape
    devices = mesh.devices.reshape(8, ctx_n // 16, 2, dp_n // 4, 4)
    fine = Mesh(devices, CTX + DP)
    return jax.shard_map(
        body,
        mesh=fine,
        in_specs=(
            P(DP, CTX, None),
            P(DP, CTX, None),
            P(DP, CTX, None),
            P(DP, CTX, None),
            P(CTX, None),
            P(None, None, CTX),
            P(CTX, None),
        ),
        out_specs=(P(DP, CTX, None), P(CTX, None)),
        check_vma=False,
    )
```

```python
import jax
import jax.numpy as jnp
from jax import lax
from jax.sharding import Mesh
from jax.sharding import PartitionSpec as P

DILATION = 32

NOISE_SCALE = 0.1

CTX = ("y", "zl", "c")
DP = ("zh", "x")


def _size(axes):
    n = 1
    for a in axes:
        n *= lax.axis_size(a)
    return n


def _swap(x, axis, d):
    n = lax.axis_size(axis)
    return lax.ppermute(x, axis, [(i, i ^ d) for i in range(n)])


def _bit(axis, d):
    return (lax.axis_index(axis) // d) % 2


DIGITS = (("y", 4), ("y", 2), ("y", 1), ("zl", 2), ("zl", 1), ("c", 1))


def _gather_rows(piece, order):
    held = piece.reshape((1,) * len(DIGITS) + piece.shape)
    for axis, d in order:
        dim = DIGITS.index((axis, d))
        theirs = _swap(held, axis, d)
        low = jnp.concatenate([held, theirs], axis=dim)
        high = jnp.concatenate([theirs, held], axis=dim)
        held = jnp.where(_bit(axis, d) == 0, low, high)
    return held.reshape((-1,) + piece.shape[1:])


def _halve(held, order):
    for axis, d in order:
        dim = DIGITS.index((axis, d))
        mine = _bit(axis, d)
        keep = lax.dynamic_index_in_dim(held, mine, axis=dim, keepdims=True)
        give = lax.dynamic_index_in_dim(held, 1 - mine, axis=dim, keepdims=True)
        held = keep + _swap(give.astype(jnp.bfloat16), axis, d).astype(held.dtype)
    return held


def _sum_all(x, steps):
    for axis, d in steps:
        x = x + _swap(x, axis, d)
    return x


def body(features, bottleneck, node_noise, targets, entry_weight, conv_filters, exit_weight):
    feats = features[0]
    bottle = bottleneck[0]
    jitter = node_noise[0]
    goal = targets[0].astype(jnp.float32)
    rows, chans = feats.shape
    bot = bottle.shape[1]
    n_ctx = _size(CTX)
    ny, nz, nc = (lax.axis_size(a) for a in CTX)
    shard = entry_weight.shape[0]

    summed = lax.dot_general(
        bottle, jitter, (((0,), (0,)), ((), ())), preferred_element_type=jnp.float32
    )

    conv_rows = conv_filters.transpose(2, 0, 1).reshape(shard, -1)
    packed = jnp.concatenate([entry_weight, conv_rows, exit_weight], axis=1)
    packed = lax.all_gather(packed, "zl", axis=0, tiled=True)
    for d in (4, 2, 1):
        packed = jnp.concatenate([packed, _swap(packed, "y", d)], axis=0)

    spacing = DILATION
    edge_in = jnp.concatenate([feats, bottle, jitter], axis=1)
    pairs_up = [(i, i + 1) for i in range(n_ctx - 1)]
    pairs_down = [(i + 1, i) for i in range(n_ctx - 1)]
    from_prev = lax.ppermute(edge_in[rows - spacing :], CTX, pairs_up)
    from_next = lax.ppermute(edge_in[:spacing], CTX, pairs_down)

    summed = summed.reshape((2,) * len(DIGITS) + (shard, chans))
    summed = _halve(summed, (("c", 1), ("zl", 1), ("zl", 2)))
    packed, summed, from_prev, from_next = lax.optimization_barrier(
        (packed, summed, from_prev, from_next)
    )
    theirs = _swap(packed, "c", 1)
    summed = _halve(summed, (("y", 1), ("y", 2), ("y", 4)))
    theirs, summed = lax.optimization_barrier((theirs, summed))
    packed = jnp.concatenate([packed, theirs], axis=0)
    summed = summed.reshape(shard, chans)
    w_entry = packed[:, :chans]
    w_conv = packed[:, chans : 4 * chans].reshape(bot, 3, chans)
    w_exit = packed[:, 4 * chans :]

    ext = jnp.concatenate([from_prev, edge_in, from_next], axis=0)
    ext_feats = ext[:, :chans]
    ys = jnp.array([int(format(p, "03b")[::-1], 2) for p in range(ny)], jnp.int32) ^ lax.axis_index("y")
    cs = jnp.arange(nc, dtype=jnp.int32) ^ lax.axis_index("c")
    ext_bottle = ext[:, chans : chans + bot].reshape(-1, ny, nz, nc, shard)
    ext_bottle = jnp.take(jnp.take(ext_bottle, ys, axis=1), cs, axis=3)
    ext_bottle = ext_bottle.transpose(0, 3, 1, 2, 4).reshape(-1, bot)
    ext_jitter = ext[:, chans + bot :]

    baseline = ext_feats.astype(jnp.float32) + jnp.dot(
        ext_bottle, w_entry, preferred_element_type=jnp.float32
    )
    offset = ext_jitter.astype(jnp.float32) * NOISE_SCALE
    state = jnp.stack([baseline + offset, baseline - offset])
    activated = jax.nn.gelu(state).astype(jnp.bfloat16)
    mixed = None
    for k in range(3):
        term = lax.dot_general(
            activated[:, k * spacing : k * spacing + rows],
            w_conv[:, k, :],
            (((2,), (1,)), ((), ())),
            preferred_element_type=jnp.float32,
        )
        mixed = term if mixed is None else mixed + term
    inner = jax.nn.gelu(mixed).astype(jnp.bfloat16)
    outs = state[:, spacing : spacing + rows] + jnp.dot(
        inner, w_exit, preferred_element_type=jnp.float32
    )
    upper = outs[0]
    lower = outs[1]
    blended = ((upper + lower) * 0.5).astype(jnp.bfloat16)[None]
    local_gap = jnp.sum((upper - lower) * (upper + lower - 2.0 * goal)) / (rows * n_ctx * chans)
    gap = local_gap
    for axis in ("c", "zl", "y"):
        gap = lax.psum(gap, axis)
    factor = gap / (2.0 * NOISE_SCALE)
    estimate = _sum_all(factor * summed, (("x", 1), ("x", 2), ("zh", 1)))
    return (blended, estimate)


def solution(mesh):
    ctx_n, dp_n = mesh.devices.shape
    devices = mesh.devices.reshape(8, ctx_n // 16, 2, dp_n // 4, 4)
    fine = Mesh(devices, CTX + DP)
    return jax.shard_map(
        body,
        mesh=fine,
        in_specs=(
            P(DP, CTX, None),
            P(DP, CTX, None),
            P(DP, CTX, None),
            P(DP, CTX, None),
            P(CTX, None),
            P(None, None, CTX),
            P(CTX, None),
        ),
        out_specs=(P(DP, CTX, None), P(CTX, None)),
        check_vma=False,
    )
```

```python
import jax
import jax.numpy as jnp
from jax import lax
from jax.sharding import Mesh
from jax.sharding import PartitionSpec as P

DILATION = 32

NOISE_SCALE = 0.1

CTX = ("y", "zl", "c")
DP = ("zh", "x")


def _size(axes):
    n = 1
    for a in axes:
        n *= lax.axis_size(a)
    return n


def _swap(x, axis, d):
    n = lax.axis_size(axis)
    return lax.ppermute(x, axis, [(i, i ^ d) for i in range(n)])


def _bit(axis, d):
    return (lax.axis_index(axis) // d) % 2


DIGITS = (("y", 4), ("y", 2), ("y", 1), ("zl", 2), ("zl", 1), ("c", 1))


def _gather_rows(piece, order):
    held = piece.reshape((1,) * len(DIGITS) + piece.shape)
    for axis, d in order:
        dim = DIGITS.index((axis, d))
        theirs = _swap(held, axis, d)
        low = jnp.concatenate([held, theirs], axis=dim)
        high = jnp.concatenate([theirs, held], axis=dim)
        held = jnp.where(_bit(axis, d) == 0, low, high)
    return held.reshape((-1,) + piece.shape[1:])


def _halve(held, order):
    for axis, d in order:
        dim = DIGITS.index((axis, d))
        mine = _bit(axis, d)
        keep = lax.dynamic_index_in_dim(held, mine, axis=dim, keepdims=True)
        give = lax.dynamic_index_in_dim(held, 1 - mine, axis=dim, keepdims=True)
        held = keep + _swap(give.astype(jnp.bfloat16), axis, d).astype(held.dtype)
    return held


def _sum_all(x, steps):
    for axis, d in steps:
        x = x + _swap(x, axis, d)
    return x


def body(features, bottleneck, node_noise, targets, entry_weight, conv_filters, exit_weight):
    feats = features[0]
    bottle = bottleneck[0]
    jitter = node_noise[0]
    goal = targets[0].astype(jnp.float32)
    rows, chans = feats.shape
    bot = bottle.shape[1]
    n_ctx = _size(CTX)
    ny, nz, nc = (lax.axis_size(a) for a in CTX)
    shard = entry_weight.shape[0]

    summed = lax.dot_general(
        bottle, jitter, (((0,), (0,)), ((), ())), preferred_element_type=jnp.float32
    )

    conv_rows = conv_filters.transpose(2, 0, 1).reshape(shard, -1)
    packed = jnp.concatenate([entry_weight, conv_rows, exit_weight], axis=1)
    for axis in ("zl", "y"):
        packed = lax.all_gather(packed, axis, axis=0, tiled=True)

    spacing = DILATION
    edge_in = jnp.concatenate([feats, bottle, jitter], axis=1)
    pairs_up = [(i, i + 1) for i in range(n_ctx - 1)]
    pairs_down = [(i + 1, i) for i in range(n_ctx - 1)]
    from_prev = lax.ppermute(edge_in[rows - spacing :], CTX, pairs_up)
    from_next = lax.ppermute(edge_in[:spacing], CTX, pairs_down)

    summed = summed.reshape((2,) * len(DIGITS) + (shard, chans))
    summed = _halve(summed, (("c", 1), ("y", 1), ("y", 2), ("y", 4)))
    packed, summed, from_prev, from_next = lax.optimization_barrier(
        (packed, summed, from_prev, from_next)
    )
    packed = lax.all_gather(packed, "c", axis=0, tiled=True)
    summed = _halve(summed, (("zl", 1), ("zl", 2)))
    packed, summed = lax.optimization_barrier((packed, summed))
    summed = summed.reshape(shard, chans)
    w_entry = packed[:, :chans]
    w_conv = packed[:, chans : 4 * chans].reshape(bot, 3, chans)
    w_exit = packed[:, 4 * chans :]

    ext = jnp.concatenate([from_prev, edge_in, from_next], axis=0)
    ext_feats = ext[:, :chans]
    ext_bottle = (
        ext[:, chans : chans + bot]
        .reshape(-1, ny, nz, nc, shard)
        .transpose(0, 3, 1, 2, 4)
        .reshape(-1, bot)
    )
    ext_jitter = ext[:, chans + bot :]

    baseline = ext_feats.astype(jnp.float32) + jnp.dot(
        ext_bottle, w_entry, preferred_element_type=jnp.float32
    )
    offset = ext_jitter.astype(jnp.float32) * NOISE_SCALE
    state = jnp.stack([baseline + offset, baseline - offset])
    activated = jax.nn.gelu(state).astype(jnp.bfloat16)
    mixed = None
    for k in range(3):
        term = lax.dot_general(
            activated[:, k * spacing : k * spacing + rows],
            w_conv[:, k, :],
            (((2,), (1,)), ((), ())),
            preferred_element_type=jnp.float32,
        )
        mixed = term if mixed is None else mixed + term
    inner = jax.nn.gelu(mixed).astype(jnp.bfloat16)
    outs = state[:, spacing : spacing + rows] + jnp.dot(
        inner, w_exit, preferred_element_type=jnp.float32
    )
    upper = outs[0]
    lower = outs[1]
    blended = ((upper + lower) * 0.5).astype(jnp.bfloat16)[None]
    local_gap = jnp.sum((upper - lower) * (upper + lower - 2.0 * goal)) / (rows * n_ctx * chans)
    gap = local_gap
    for axis in ("c", "zl", "y"):
        gap = lax.psum(gap, axis)
    factor = gap / (2.0 * NOISE_SCALE)
    estimate = _sum_all(factor * summed, (("x", 1), ("x", 2), ("zh", 1)))
    return (blended, estimate)


def solution(mesh):
    ctx_n, dp_n = mesh.devices.shape
    devices = mesh.devices.reshape(8, ctx_n // 16, 2, dp_n // 4, 4)
    fine = Mesh(devices, CTX + DP)
    return jax.shard_map(
        body,
        mesh=fine,
        in_specs=(
            P(DP, CTX, None),
            P(DP, CTX, None),
            P(DP, CTX, None),
            P(DP, CTX, None),
            P(CTX, None),
            P(None, None, CTX),
            P(CTX, None),
        ),
        out_specs=(P(DP, CTX, None), P(CTX, None)),
        check_vma=False,
    )
```

```python
import jax
import jax.numpy as jnp
from jax import lax
from jax.sharding import Mesh
from jax.sharding import PartitionSpec as P

DILATION = 32

NOISE_SCALE = 0.1

CTX = ("y", "zl", "c")
DP = ("zh", "x")


def _size(axes):
    n = 1
    for a in axes:
        n *= lax.axis_size(a)
    return n


def _swap(x, axis, d):
    n = lax.axis_size(axis)
    return lax.ppermute(x, axis, [(i, i ^ d) for i in range(n)])


def _bit(axis, d):
    return (lax.axis_index(axis) // d) % 2


DIGITS = (("y", 4), ("y", 2), ("y", 1), ("zl", 2), ("zl", 1), ("c", 1))


def _gather_rows(piece, order):
    held = piece.reshape((1,) * len(DIGITS) + piece.shape)
    for axis, d in order:
        dim = DIGITS.index((axis, d))
        theirs = _swap(held, axis, d)
        low = jnp.concatenate([held, theirs], axis=dim)
        high = jnp.concatenate([theirs, held], axis=dim)
        held = jnp.where(_bit(axis, d) == 0, low, high)
    return held.reshape((-1,) + piece.shape[1:])


def _halve(held, order):
    for axis, d in order:
        dim = DIGITS.index((axis, d))
        mine = _bit(axis, d)
        keep = lax.dynamic_index_in_dim(held, mine, axis=dim, keepdims=True)
        give = lax.dynamic_index_in_dim(held, 1 - mine, axis=dim, keepdims=True)
        held = keep + _swap(give.astype(jnp.bfloat16), axis, d).astype(held.dtype)
    return held


def _sum_all(x, steps):
    for axis, d in steps:
        x = x + _swap(x, axis, d)
    return x


def body(features, bottleneck, node_noise, targets, entry_weight, conv_filters, exit_weight):
    feats = features[0]
    bottle = bottleneck[0]
    jitter = node_noise[0]
    goal = targets[0].astype(jnp.float32)
    rows, chans = feats.shape
    bot = bottle.shape[1]
    n_ctx = _size(CTX)
    ny, nz, nc = (lax.axis_size(a) for a in CTX)
    shard = entry_weight.shape[0]

    summed = lax.dot_general(
        bottle, jitter, (((0,), (0,)), ((), ())), preferred_element_type=jnp.float32
    )

    conv_rows = conv_filters.transpose(2, 0, 1).reshape(shard, -1)
    packed = jnp.concatenate([entry_weight, conv_rows, exit_weight], axis=1)
    for axis in ("zl", "y"):
        packed = lax.all_gather(packed, axis, axis=0, tiled=True)

    spacing = DILATION
    edge_in = jnp.concatenate([feats, bottle, jitter], axis=1)
    pairs_up = [(i, i + 1) for i in range(n_ctx - 1)]
    pairs_down = [(i + 1, i) for i in range(n_ctx - 1)]
    from_prev = lax.ppermute(edge_in[rows - spacing :], CTX, pairs_up)
    from_next = lax.ppermute(edge_in[:spacing], CTX, pairs_down)

    summed = summed.reshape((2,) * len(DIGITS) + (shard, chans))
    summed = _halve(summed, (("c", 1), ("zl", 1), ("zl", 2)))
    packed, summed, from_prev, from_next = lax.optimization_barrier(
        (packed, summed, from_prev, from_next)
    )
    packed = lax.all_gather(packed, "c", axis=0, tiled=True)
    summed = _halve(summed, (("y", 1), ("y", 2), ("y", 4)))
    packed, summed = lax.optimization_barrier((packed, summed))
    summed = summed.reshape(shard, chans)
    w_entry = packed[:, :chans]
    w_conv = packed[:, chans : 4 * chans].reshape(bot, 3, chans)
    w_exit = packed[:, 4 * chans :]

    ext = jnp.concatenate([from_prev, edge_in, from_next], axis=0)
    ext_feats = ext[:, :chans]
    ext_bottle = (
        ext[:, chans : chans + bot]
        .reshape(-1, ny, nz, nc, shard)
        .transpose(0, 3, 1, 2, 4)
        .reshape(-1, bot)
    )
    ext_jitter = ext[:, chans + bot :]

    baseline = ext_feats.astype(jnp.float32) + jnp.dot(
        ext_bottle, w_entry, preferred_element_type=jnp.float32
    )
    offset = ext_jitter.astype(jnp.float32) * NOISE_SCALE
    state = jnp.stack([baseline + offset, baseline - offset])
    activated = jax.nn.gelu(state).astype(jnp.bfloat16)
    mixed = None
    for k in range(3):
        term = lax.dot_general(
            activated[:, k * spacing : k * spacing + rows],
            w_conv[:, k, :],
            (((2,), (1,)), ((), ())),
            preferred_element_type=jnp.float32,
        )
        mixed = term if mixed is None else mixed + term
    inner = jax.nn.gelu(mixed).astype(jnp.bfloat16)
    outs = state[:, spacing : spacing + rows] + jnp.dot(
        inner, w_exit, preferred_element_type=jnp.float32
    )
    upper = outs[0]
    lower = outs[1]
    blended = ((upper + lower) * 0.5).astype(jnp.bfloat16)[None]
    local_gap = jnp.sum((upper - lower) * (upper + lower - 2.0 * goal)) / (rows * n_ctx * chans)
    gap = lax.psum(lax.psum(local_gap, ("zl", "c")), "y")
    factor = gap / (2.0 * NOISE_SCALE)
    estimate = _sum_all(factor * summed, (("x", 1), ("x", 2), ("zh", 1)))
    return (blended, estimate)


def solution(mesh):
    ctx_n, dp_n = mesh.devices.shape
    devices = mesh.devices.reshape(8, ctx_n // 16, 2, dp_n // 4, 4)
    fine = Mesh(devices, CTX + DP)
    return jax.shard_map(
        body,
        mesh=fine,
        in_specs=(
            P(DP, CTX, None),
            P(DP, CTX, None),
            P(DP, CTX, None),
            P(DP, CTX, None),
            P(CTX, None),
            P(None, None, CTX),
            P(CTX, None),
        ),
        out_specs=(P(DP, CTX, None), P(CTX, None)),
        check_vma=False,
    )
```
